256 devices in a mesh: seq: 32 (over x, y, z_hi), tp: 8 (over z_lo, core).
Axes of the slice: x: 4, y: 4, z: 8 (z_hi: 2, z_lo: 4; z = z_hi * 4 + z_lo), core: 2. Of those that a mesh axis runs over, the one named last changes fastest.
Arguments:
- prefill_tokens: bfloat16 [8192, 4608], P('seq'), may hold values from -6 to 6
- decode_tokens: bfloat16 [64, 4608], replicated, may hold values from -6 to 6
- norm_gain: float32 [4608], replicated, may hold values from 0.1 to 1.9
- w_query: bfloat16 [4608, 4096], P('seq', 'tp'), may hold values from -2.1213203 to 2.1213203
- w_key: bfloat16 [4608, 2048], P('seq', 'tp'), may hold values from -0.09375 to 0.09375
- w_value: bfloat16 [4608, 2048], P('seq', 'tp'), may hold values from -0.09375 to 0.09375
- w_output: bfloat16 [4096, 4608], P('seq', 'tp'), may hold values from -0.09375 to 0.09375
- prefill_lengths: int32 [6], replicated, may hold values from 1 to 6144, 8192 in all
- context_lengths: int32 [2], replicated, may hold values from 2048 to 8192, as said below
- tail_lengths: int32 [32], replicated, may hold values from 1 to 256, as said below
- tail_slots: int32 [32], replicated, may hold values from 0 to 63, as said below
- cache_keys: bfloat16 [2, 8192, 2048], P(None, 'seq', 'tp'), may hold values from -6 to 6
- cache_values: bfloat16 [2, 8192, 2048], P(None, 'seq', 'tp'), may hold values from -6 to 6
- tail_keys: bfloat16 [64, 256, 2048], P('seq', None, 'tp'), may hold values from -6 to 6
- tail_values: bfloat16 [64, 256, 2048], P('seq', None, 'tp'), may hold values from -6 to 6
Outputs:
- prefill_out: bfloat16 [8192, 4608], P('seq', 'tp')
- decode_out: bfloat16 [64, 4608], P('seq', 'tp')
The draws below stay inside these ranges and needn't reach their ends.
Inputs may be any that keep to these rules, and one draw needn't show every extreme that they name: `prefill_lengths`: the prompts fill all 8192 prefill tokens; the longest has exactly 6144. `context_lengths`: some prompt has exactly 8192 cached positions. `tail_lengths`: some sample has exactly 256 tail positions. `tail_slots`: distinct slot numbers; slot q lies with seq index q // 2; in every draw all slots of some seq index are used.
All inputs are finite; a program needn't handle non-finite values.
Results may differ from the reference program's by a relative error of at most 0.019.
Values may be sent and summed in bfloat16 or wider, within the bound.
No kernel may reach another device: no remote copies, remote signals or barrier semaphores. Data moves between devices by JAX's collectives and lax.ppermute only.
A program may use at most 128 MiB of HBM per device.

```python
import math
import jax
import jax.numpy as jnp
import numpy as np
from jax import lax

D = 4608
HEADS = 32
KV_HEADS = 16
HEAD = 128
PF_PROMPTS = 6
PROMPTS = 2
SAMPLES = 16
NEW = 2
TAIL = 256
TOKENS_PF = 8192
CTX = 8192
DEC_ROWS = 64
SLOTS = 64


def draw_w_query(key, part):
    entry_key, level_key, sharp_key = jax.random.split(jax.random.fold_in(key, 41), 3)
    entries = jnp.clip(jax.random.normal(entry_key, (D, HEADS, HEAD), jnp.float32), -6.0, 6.0)
    levels = jax.random.uniform(level_key, (HEADS,), jnp.float32, 0.0, 1.0)
    sharpest = jax.random.randint(sharp_key, (), 0, HEADS)
    levels = jnp.where(jnp.arange(HEADS) == sharpest, 1.0, levels)
    head_scale = jnp.exp(levels * math.log(24.0))
    scaled = entries * head_scale[None, :, None] * float(D) ** (-0.5)
    return scaled.reshape(D, HEADS * HEAD).astype(jnp.bfloat16)


def draw_context_lengths(key, part):
    first_key, second_key = jax.random.split(jax.random.fold_in(key, 11))
    drawn = jax.random.randint(first_key, (PROMPTS,), CTX // 4, CTX + 1)
    longest = jax.random.randint(second_key, (), 0, PROMPTS)
    return jnp.where(jnp.arange(PROMPTS) == longest, CTX, drawn).astype(jnp.int32)


def draw_tail_lengths(key, part):
    first_key, second_key = jax.random.split(jax.random.fold_in(key, 23))
    drawn = jax.random.randint(first_key, (PROMPTS * SAMPLES,), 1, TAIL + 1)
    longest = jax.random.randint(second_key, (), 0, PROMPTS * SAMPLES)
    return jnp.where(jnp.arange(PROMPTS * SAMPLES) == longest, TAIL, drawn).astype(jnp.int32)


def draw_tail_slots(key, part):
    first_key, second_key, third_key = jax.random.split(jax.random.fold_in(key, 37), 3)
    filled_device = jax.random.randint(first_key, (), 0, SLOTS // PROMPTS)
    ranking = jax.random.permutation(second_key, SLOTS)
    slot_ids = jnp.arange(SLOTS)
    priority = ranking + jnp.where(slot_ids // PROMPTS == filled_device, -SLOTS, 0)
    chosen = jnp.argsort(priority, stable=True)[:PROMPTS * SAMPLES]
    return jax.random.permutation(third_key, chosen).astype(jnp.int32)


def level_of(own_key, shape, cuts, low, top_value):
    gain, own = 1.0, jax.random.fold_in(own_key, 6)
    for axis_at, blocks in cuts:
        heights = jnp.exp(jax.random.uniform(jax.random.fold_in(own, axis_at), (blocks,), jnp.float32, low / len(cuts), top_value / len(cuts)))
        gain = gain * jnp.repeat(heights, shape[axis_at] // blocks).reshape([-1 if axis == axis_at else 1 for axis in range(len(shape))])
    return gain


def length_profile(number_of, total, reach, skew):
    loads = [(1 << 20) // math.isqrt(standing ** skew) + 1 for standing in range(2, number_of + 1)]
    rest, holding = total - reach - (number_of - 1), [1] * (number_of - 1)
    while rest > 0:
        free = [i for i in range(number_of - 1) if holding[i] < reach]
        whole, left = sum([loads[i] for i in free]), rest
        for i in free:
            extra = min(reach - holding[i], max(1, left * loads[i] // whole), rest)
            holding[i] = holding[i] + extra
            rest = rest - extra
    return np.array([reach] + holding)


def uneven(stream_key, number_of, total, bound, slope):
    if number_of == 2:
        one = jax.random.randint(stream_key, (), max(1, total - bound), min(bound, total - 1) + 1)
        return jnp.stack([one, total - one])
    lengths = jnp.asarray(length_profile(number_of, total, bound, slope), jnp.int32)
    twos = (number_of - 1) // 2
    source_of, receiver = lengths[1:1 + 2 * twos:2], lengths[2:2 + 2 * twos:2]
    slack = jnp.minimum(source_of - 1, bound - receiver)
    shifted = jax.random.randint(jax.random.fold_in(stream_key, 1), (twos,), 0, 1 << 20) % (slack + 1)
    lengths = lengths.at[1:1 + 2 * twos:2].set(source_of - shifted).at[2:2 + 2 * twos:2].set(receiver + shifted)
    return lengths[jax.random.permutation(jax.random.fold_in(stream_key, 2), number_of)]


def normal_values(key, shape, width, bound, shards=(), kind=jnp.bfloat16):
    values = jax.random.normal(key, shape, jnp.float32) * width
    if len(shards) > 0:
        values = level_of(key, shape, shards, -0.22, 0.18) * values
    return jnp.clip(values, min=-bound, max=bound).astype(kind)


def setup_inputs(seed: int = 0) -> dict:
    key_of = jax.random.split(jax.random.key(seed), 16)
    prefill_tokens = normal_values(key_of[0], (TOKENS_PF, D), 1.0, 6.0, ((0, 32),))
    decode_tokens = normal_values(key_of[1], (DEC_ROWS, D), 1.0, 6.0)
    norm_gain = jnp.clip(1.0 + 0.18 * jax.random.normal(key_of[2], (D,), jnp.float32), 0.1, 1.9)
    w_query = draw_w_query(jax.random.fold_in(key_of[15], 71), 0)
    w_key = normal_values(key_of[4], (D, KV_HEADS * HEAD), D ** -0.5, 0.09375, ((0, 32), (1, 8)))
    w_value = normal_values(key_of[5], (D, KV_HEADS * HEAD), D ** -0.5, 0.09375, ((0, 32), (1, 8)))
    w_output = normal_values(key_of[6], (HEADS * HEAD, D), (HEADS * HEAD) ** -0.5, 0.09375, ((0, 32), (1, 8)))
    prefill_lengths = uneven(key_of[7], PF_PROMPTS, TOKENS_PF, TOKENS_PF * 3 // 4, 2).astype(jnp.int32)
    context_lengths = draw_context_lengths(jax.random.fold_in(key_of[15], 71), 0)
    tail_lengths = draw_tail_lengths(jax.random.fold_in(key_of[15], 71), 0)
    tail_slots = draw_tail_slots(jax.random.fold_in(key_of[15], 71), 0)
    cache_keys = normal_values(key_of[11], (PROMPTS, CTX, KV_HEADS * HEAD), 1.0, 6.0, ((1, 32), (2, 8)))
    cache_values = normal_values(key_of[12], (PROMPTS, CTX, KV_HEADS * HEAD), 1.0, 6.0, ((1, 32), (2, 8)))
    tail_keys = normal_values(key_of[13], (SLOTS, TAIL, KV_HEADS * HEAD), 1.0, 6.0, ((0, 32), (2, 8)))
    tail_values = normal_values(key_of[14], (SLOTS, TAIL, KV_HEADS * HEAD), 1.0, 6.0, ((0, 32), (2, 8)))
    return {"prefill_tokens": prefill_tokens, "decode_tokens": decode_tokens, "norm_gain": norm_gain, "w_query": w_query, "w_key": w_key, "w_value": w_value, "w_output": w_output, "prefill_lengths": prefill_lengths, "context_lengths": context_lengths, "tail_lengths": tail_lengths, "tail_slots": tail_slots, "cache_keys": cache_keys, "cache_values": cache_values, "tail_keys": tail_keys, "tail_values": tail_values}


SOFTCAP = 50.0
QUERY_SCALE = 144.0 ** (-0.5)
NORM_EPSILON = 1e-06
ROPE_BASE = 10000.0

def rms_norm(inputs, norm_gain):
    values = inputs.astype(jnp.float32)
    mean_sq = lax.optimization_barrier(jnp.mean(values * values, axis=-1, keepdims=True))
    return (values * lax.rsqrt(mean_sq + NORM_EPSILON) * norm_gain.astype(jnp.float32)).astype(jnp.bfloat16)

def rotate(values, positions):
    half_size = values.shape[-1] // 2
    exponent = jnp.arange(half_size, dtype=jnp.float32) * (2.0 / values.shape[-1])
    frequency = ROPE_BASE ** (-exponent)
    angles = positions.astype(jnp.float32)[:, None] * frequency[None, :]
    cosine = jnp.cos(angles)[:, None, :]
    sine_part = jnp.sin(angles)[:, None, :]
    lower_half = values[..., :half_size]
    upper_half = values[..., half_size:]
    return jnp.concatenate([lower_half * cosine - upper_half * sine_part, upper_half * cosine + lower_half * sine_part], axis=-1)

def project(normed, w_query, w_key, w_value, positions):
    row_count = normed.shape[0]
    query_rows = jnp.dot(normed, w_query, preferred_element_type=jnp.float32).reshape(row_count, -1, HEAD)
    key_rows = jnp.dot(normed, w_key, preferred_element_type=jnp.float32).reshape(row_count, -1, HEAD)
    value_rows = jnp.dot(normed, w_value, preferred_element_type=jnp.float32)
    query_rows = (rotate(query_rows, positions) * QUERY_SCALE).astype(jnp.bfloat16).reshape(row_count, -1)
    key_rows = rotate(key_rows, positions).astype(jnp.bfloat16).reshape(row_count, -1)
    return (query_rows, key_rows, value_rows.astype(jnp.bfloat16))

def soft_cap(scores):
    return SOFTCAP * jnp.tanh(scores / SOFTCAP)

def prefill_positions(prefill_lengths, token_index):
    prompt_ends = jnp.cumsum(prefill_lengths).astype(jnp.int32)
    passed = token_index[:, None] >= prompt_ends[None, :]
    segment = lax.optimization_barrier(jnp.sum(passed.astype(jnp.int32), axis=1)).astype(jnp.int32)
    start_at = lax.optimization_barrier(jnp.sum(jnp.where(passed, prefill_lengths[None, :], 0), axis=1)).astype(jnp.int32)
    return (segment, token_index - start_at)

def lookup(table, indices):
    entries = jnp.arange(table.shape[0], dtype=jnp.int32)
    return lax.optimization_barrier(jnp.sum(jnp.where(indices[:, None] == entries[None, :], table[None, :], 0), axis=1)).astype(jnp.int32)

def decode_positions(context_lengths, tail_lengths, row_ids):
    sample_ids = row_ids // NEW
    prompt_ids = sample_ids // SAMPLES
    return lookup(context_lengths, prompt_ids) + lookup(tail_lengths, sample_ids) + row_ids % NEW

def prefill_attention(query_rows, key_rows, value_rows, segment, token_index):
    tokens = query_rows.shape[0]
    group_size = HEADS // KV_HEADS
    queries = query_rows.astype(jnp.float32).reshape(tokens, KV_HEADS, group_size, HEAD).transpose(1, 0, 2, 3)
    keys_all = key_rows.astype(jnp.float32).reshape(tokens, KV_HEADS, HEAD).transpose(1, 0, 2)
    values_all = value_rows.astype(jnp.float32).reshape(tokens, KV_HEADS, HEAD).transpose(1, 0, 2)
    block_len = math.gcd(512, tokens)

    def per_group(operands):
        group_queries, group_keys, group_values = operands

        def per_block(block_index):
            start_at = block_index * block_len
            query_part = lax.dynamic_slice_in_dim(group_queries, start_at, block_len, 0)
            query_seg = lax.dynamic_slice_in_dim(segment, start_at, block_len, 0)
            query_idx = lax.dynamic_slice_in_dim(token_index, start_at, block_len, 0)
            allowed = (query_seg[:, None] == segment[None, :]) & (token_index[None, :] <= query_idx[:, None])
            allowed = allowed[:, None, :]
            scores = soft_cap(jnp.einsum('qjd,kd->qjk', query_part, group_keys))
            weights = jnp.where(allowed, jnp.exp(scores), 0.0)
            total_sum = lax.optimization_barrier(jnp.sum(weights, axis=-1))
            mixed_out = jnp.einsum('qjk,kd->qjd', weights.astype(jnp.bfloat16).astype(jnp.float32), group_values)
            return mixed_out / total_sum[..., None]
        return lax.map(per_block, jnp.arange(tokens // block_len, dtype=jnp.int32))
    attended = lax.map(per_group, (queries, keys_all, values_all))
    return attended.transpose(1, 2, 0, 3, 4).reshape(tokens, HEADS * HEAD).astype(jnp.bfloat16)

def decode_attention(query_rows, key_rows, value_rows, context_lengths, tail_lengths, tail_slots, cache_keys, cache_values, tail_keys, tail_values):
    group_size = HEADS // KV_HEADS
    queries = query_rows.astype(jnp.float32).reshape(PROMPTS, SAMPLES, NEW, KV_HEADS, group_size, HEAD)
    new_keys = key_rows.astype(jnp.float32).reshape(PROMPTS, SAMPLES, NEW, KV_HEADS, HEAD)
    new_values = value_rows.astype(jnp.float32).reshape(PROMPTS, SAMPLES, NEW, KV_HEADS, HEAD)
    slot_table = tail_slots.reshape(PROMPTS, SAMPLES)
    tail_table = tail_lengths.reshape(PROMPTS, SAMPLES)
    cache_pos = jnp.arange(CTX, dtype=jnp.int32)
    tail_pos = jnp.arange(TAIL, dtype=jnp.int32)
    new_pos = jnp.arange(NEW, dtype=jnp.int32)
    new_allowed = (new_pos[None, :] <= new_pos[:, None])[None, :, None, None, :]

    def per_prompt(operands):
        prompt_queries, prompt_keys, prompt_values, context_len, slot_row, tail_row, prompt_ck, prompt_cv = operands
        cache_k = prompt_ck.astype(jnp.float32).reshape(CTX, KV_HEADS, HEAD)
        cache_v = prompt_cv.astype(jnp.float32).reshape(CTX, KV_HEADS, HEAD)
        slot_keys = jnp.take(tail_keys, slot_row, axis=0).astype(jnp.float32).reshape(SAMPLES, TAIL, KV_HEADS, HEAD)
        slot_values = jnp.take(tail_values, slot_row, axis=0).astype(jnp.float32).reshape(SAMPLES, TAIL, KV_HEADS, HEAD)
        cache_allowed = (cache_pos < context_len)[None, None, None, None, :]
        tail_allowed = (tail_pos[None, :] < tail_row[:, None])[:, None, None, None, :]
        cache_weights = jnp.where(cache_allowed, jnp.exp(soft_cap(jnp.einsum('sngjd,cgd->sngjc', prompt_queries, cache_k))), 0.0)
        tail_weights = jnp.where(tail_allowed, jnp.exp(soft_cap(jnp.einsum('sngjd,stgd->sngjt', prompt_queries, slot_keys))), 0.0)
        new_weights = jnp.where(new_allowed, jnp.exp(soft_cap(jnp.einsum('sngjd,smgd->sngjm', prompt_queries, prompt_keys))), 0.0)
        total_sum = cache_weights.sum(-1) + tail_weights.sum(-1) + new_weights.sum(-1)
        mixed_out = jnp.einsum('sngjc,cgd->sngjd', cache_weights.astype(jnp.bfloat16).astype(jnp.float32), cache_v)
        mixed_out = mixed_out + jnp.einsum('sngjt,stgd->sngjd', tail_weights.astype(jnp.bfloat16).astype(jnp.float32), slot_values)
        mixed_out = mixed_out + jnp.einsum('sngjm,smgd->sngjd', new_weights.astype(jnp.bfloat16).astype(jnp.float32), prompt_values)
        return mixed_out / total_sum[..., None]
    attended = lax.map(per_prompt, (queries, new_keys, new_values, context_lengths, slot_table, tail_table, cache_keys, cache_values))
    return attended.reshape(PROMPTS * SAMPLES * NEW, HEADS * HEAD).astype(jnp.bfloat16)

def reference(prefill_tokens, decode_tokens, norm_gain, w_query, w_key, w_value, w_output, prefill_lengths, context_lengths, tail_lengths, tail_slots, cache_keys, cache_values, tail_keys, tail_values):
    token_index = jnp.arange(TOKENS_PF, dtype=jnp.int32)
    segment, pf_positions = prefill_positions(prefill_lengths, token_index)
    pf_query, pf_key, pf_value = project(rms_norm(prefill_tokens, norm_gain), w_query, w_key, w_value, pf_positions)
    pf_attn = prefill_attention(pf_query, pf_key, pf_value, segment, token_index)
    prefill_out = jnp.dot(pf_attn, w_output, preferred_element_type=jnp.float32).astype(jnp.bfloat16)
    row_ids = jnp.arange(DEC_ROWS, dtype=jnp.int32)
    dec_positions = decode_positions(context_lengths, tail_lengths, row_ids)
    dec_query, dec_key, dec_value = project(rms_norm(decode_tokens, norm_gain), w_query, w_key, w_value, dec_positions)
    dec_attn = decode_attention(dec_query, dec_key, dec_value, context_lengths, tail_lengths, tail_slots, cache_keys, cache_values, tail_keys, tail_values)
    decode_out = jnp.dot(dec_attn, w_output, preferred_element_type=jnp.float32).astype(jnp.bfloat16)
    return (prefill_out, decode_out)
```

```python
import math

import jax
import jax.numpy as jnp
from jax import lax
from jax.sharding import PartitionSpec as P

HEAD = 128
SAMPLES = 16
NEW = 2


SOFTCAP = 50.0
QUERY_SCALE = 144.0 ** (-0.5)
NORM_EPSILON = 1e-06
ROPE_BASE = 10000.0


def rows_of(x, width):
    flat = x.reshape(-1).astype(jnp.bfloat16)
    tile = width * 16
    padded = -(-flat.shape[0] // tile) * tile
    return jnp.pad(flat, (0, padded - flat.shape[0])).reshape(-1, width)


def unrows(gathered, shape):
    count = gathered.shape[0]
    size = math.prod(shape)
    flat = gathered.reshape(count, -1)[:, :size].astype(jnp.float32)
    return jnp.sum(flat, axis=0).reshape(shape)


def rms_norm(inputs, norm_gain):
    values = inputs.astype(jnp.float32)
    mean_sq = jnp.mean(values * values, axis=-1, keepdims=True)
    return (values * lax.rsqrt(mean_sq + NORM_EPSILON) * norm_gain).astype(jnp.bfloat16)


def rotate(values, positions):
    half_size = values.shape[-1] // 2
    exponent = jnp.arange(half_size, dtype=jnp.float32) * (2.0 / values.shape[-1])
    frequency = ROPE_BASE ** (-exponent)
    angles = positions.astype(jnp.float32)[:, None] * frequency[None, :]
    cosine = jnp.cos(angles)[:, None, :]
    sine_part = jnp.sin(angles)[:, None, :]
    lower_half = values[..., :half_size]
    upper_half = values[..., half_size:]
    return jnp.concatenate(
        [
            lower_half * cosine - upper_half * sine_part,
            upper_half * cosine + lower_half * sine_part,
        ],
        axis=-1,
    )


def soft_cap(scores):
    return SOFTCAP * jnp.tanh(scores / SOFTCAP)


def prefill_positions(prefill_lengths, token_index):
    prompt_ends = jnp.cumsum(prefill_lengths)
    passed = token_index[:, None] >= prompt_ends[None, :]
    segment = jnp.sum(passed.astype(jnp.int32), axis=1)
    start_at = jnp.sum(jnp.where(passed, prefill_lengths[None, :], 0), axis=1)
    return (segment, token_index - start_at)


def lookup(table, indices):
    entries = jnp.arange(table.shape[0], dtype=jnp.int32)
    return jnp.sum(jnp.where(indices[:, None] == entries[None, :], table[None, :], 0), axis=1)


def combine(earlier, later):
    return (earlier[0] + later[0], earlier[1] + later[1])


def partial_softmax(scores, allowed, value_block, form):
    weights = jnp.where(allowed, jnp.exp(scores), 0.0)
    total_sum = jnp.sum(weights, axis=-1)
    mixed_out = jnp.einsum(
        form, weights.astype(jnp.bfloat16), value_block, preferred_element_type=jnp.float32
    )
    return (total_sum, mixed_out)


def shards(
    prefill_tokens,
    decode_tokens,
    norm_gain,
    w_query,
    w_key,
    w_value,
    w_output,
    prefill_lengths,
    context_lengths,
    tail_lengths,
    tail_slots,
    cache_keys,
    cache_values,
    tail_keys,
    tail_values,
):
    seq_count = lax.axis_size("seq")
    seq_index = lax.axis_index("seq")
    pf_rows = prefill_tokens.shape[0]
    dec_total = decode_tokens.shape[0]
    dec_rows = dec_total // seq_count
    q_heads = w_query.shape[1] // HEAD
    kv_heads = w_key.shape[1] // HEAD
    group_size = q_heads // kv_heads
    token_index = seq_index * pf_rows + jnp.arange(pf_rows, dtype=jnp.int32)
    query_seg, pf_positions = prefill_positions(prefill_lengths, token_index)
    row_ids = jnp.arange(dec_total, dtype=jnp.int32)
    sample_ids = row_ids // NEW
    dec_positions = (
        lookup(context_lengths, sample_ids // SAMPLES)
        + lookup(tail_lengths, sample_ids)
        + row_ids % NEW
    )
    positions = jnp.concatenate([pf_positions, dec_positions], axis=0)
    normed = rms_norm(jnp.concatenate([prefill_tokens, decode_tokens], axis=0), norm_gain)
    row_total = normed.shape[0]
    q_cols = w_query.shape[1]
    k_cols = w_key.shape[1]
    w_rows = w_query.shape[0]
    qkv_local = jnp.concatenate([w_query, w_key, w_value], axis=1)
    qkv_cols = qkv_local.shape[1]
    o_rows, o_cols = w_output.shape
    packed_w = jnp.concatenate([qkv_local, w_output.reshape(-1, qkv_cols)], axis=0)
    gathered_w = lax.all_gather(packed_w, "seq", axis=0)
    w_qkv = gathered_w[:, :w_rows].reshape(seq_count * w_rows, qkv_cols)
    w_out = gathered_w[:, w_rows:].reshape(seq_count * o_rows, o_cols)
    qkv_all = jnp.dot(normed, w_qkv, preferred_element_type=jnp.float32)
    query_all = qkv_all[:, :q_cols]
    key_all = qkv_all[:, q_cols:q_cols + k_cols]
    value_all = qkv_all[:, q_cols + k_cols:]
    query_all = (
        rotate(query_all.reshape(row_total, q_heads, HEAD), positions) * QUERY_SCALE
    ).astype(jnp.bfloat16)
    key_all = (
        rotate(key_all.reshape(row_total, kv_heads, HEAD), positions)
        .astype(jnp.bfloat16)
        .reshape(row_total, -1)
    )
    value_all = value_all.astype(jnp.bfloat16)
    pf_query = query_all[:pf_rows].reshape(pf_rows, kv_heads, group_size, HEAD)
    pf_key = key_all[:pf_rows]
    pf_value = value_all[:pf_rows]
    dec_query = query_all[pf_rows:]
    dec_key = key_all[pf_rows:]
    dec_value = value_all[pf_rows:]
    prompt_count = cache_keys.shape[0]
    ctx_rows = cache_keys.shape[1]
    prompt_queries = dec_query.reshape(prompt_count, SAMPLES * NEW, kv_heads, group_size, HEAD)
    cache_k = cache_keys.reshape(prompt_count, ctx_rows, kv_heads, HEAD)
    cache_v = cache_values.reshape(prompt_count, ctx_rows, kv_heads, HEAD)
    cache_pos = seq_index * ctx_rows + jnp.arange(ctx_rows, dtype=jnp.int32)
    cache_allowed = (cache_pos[None, :] < context_lengths[:, None])[:, None, None, None, :]
    cache_scores = soft_cap(
        jnp.einsum("prgjd,pcgd->prgjc", prompt_queries, cache_k, preferred_element_type=jnp.float32)
    )
    prefix_part = partial_softmax(cache_scores, cache_allowed, cache_v, "prgjc,pcgd->prgjd")
    prefix_part = (
        prefix_part[0].reshape(dec_total, kv_heads, group_size),
        prefix_part[1].reshape(dec_total, kv_heads, group_size, HEAD),
    )
    slot_count = tail_keys.shape[0]
    tail_len = tail_keys.shape[1]
    sample_total = tail_slots.shape[0]
    local_slots = seq_index * slot_count + jnp.arange(slot_count, dtype=jnp.int32)
    owner = tail_slots[None, :] == local_slots[:, None]
    slot_queries = jnp.dot(
        owner.astype(jnp.bfloat16),
        dec_query.reshape(sample_total, NEW * q_heads * HEAD),
        preferred_element_type=jnp.float32,
    )
    slot_queries = slot_queries.astype(jnp.bfloat16).reshape(
        slot_count, NEW, kv_heads, group_size, HEAD
    )
    slot_lengths = jnp.sum(jnp.where(owner, tail_lengths[None, :], 0), axis=1)
    tail_allowed = (jnp.arange(tail_len, dtype=jnp.int32)[None, :] < slot_lengths[:, None])[
        :, None, None, None, :
    ]
    slot_keys = tail_keys.reshape(slot_count, tail_len, kv_heads, HEAD)
    slot_values = tail_values.reshape(slot_count, tail_len, kv_heads, HEAD)
    tail_scores = soft_cap(
        jnp.einsum("sngjd,stgd->sngjt", slot_queries, slot_keys, preferred_element_type=jnp.float32)
    )
    slot_part = partial_softmax(tail_scores, tail_allowed, slot_values, "sngjt,stgd->sngjd")
    owned_by = owner.T
    tail_sum = jnp.sum(jnp.where(owned_by[:, :, None, None, None], slot_part[0][None], 0.0), axis=1)
    tail_mix = jnp.sum(
        jnp.where(owned_by[:, :, None, None, None, None], slot_part[1][None], 0.0), axis=1
    )
    tail_part = (
        tail_sum.reshape(dec_total, kv_heads, group_size),
        tail_mix.reshape(dec_total, kv_heads, group_size, HEAD),
    )
    partials = combine(prefix_part, tail_part)
    kv_local = jnp.concatenate([pf_key, pf_value], axis=1)
    width = kv_local.shape[1]
    packed_kv = jnp.concatenate(
        [kv_local, rows_of(partials[1], width), rows_of(partials[0], width)], axis=0
    )
    gathered_kv = lax.all_gather(packed_kv, "seq", axis=0)
    piece_len = pf_rows * seq_count
    key_piece = gathered_kv[:, :pf_rows, :k_cols].reshape(piece_len, k_cols)
    value_piece = gathered_kv[:, :pf_rows, k_cols:].reshape(piece_len, k_cols)
    mix_rows = rows_of(partials[1], width).shape[0]
    combined = (
        unrows(gathered_kv[:, pf_rows + mix_rows:], partials[0].shape),
        unrows(gathered_kv[:, pf_rows:pf_rows + mix_rows], partials[1].shape),
    )
    query_last = token_index[pf_rows - 1]
    prompt_first = token_index[0] - pf_positions[0]
    start_state = (
        jnp.zeros((pf_rows, kv_heads, group_size), jnp.float32),
        jnp.zeros((pf_rows, kv_heads, group_size, HEAD), jnp.float32),
    )
    block_len = math.gcd(512, piece_len)

    def one_block(block_step, carry_state):
        begin = block_step * block_len
        key_block = lax.dynamic_slice_in_dim(
            key_piece, block_step * block_len, block_len, 0
        ).reshape(block_len, kv_heads, HEAD)
        value_block = lax.dynamic_slice_in_dim(
            value_piece, block_step * block_len, block_len, 0
        ).reshape(block_len, kv_heads, HEAD)

        def compute(state_in):
            key_index = begin + jnp.arange(block_len, dtype=jnp.int32)
            key_seg, unused_pos = prefill_positions(prefill_lengths, key_index)
            allowed = (query_seg[:, None] == key_seg[None, :]) & (
                key_index[None, :] <= token_index[:, None]
            )
            scores = soft_cap(
                jnp.einsum(
                    "qgjd,kgd->qgjk", pf_query, key_block, preferred_element_type=jnp.float32
                )
            )
            weights = jnp.where(allowed[:, None, None, :], jnp.exp(scores), 0.0)
            total_sum = state_in[0] + jnp.sum(weights, axis=-1)
            mixed_out = state_in[1] + jnp.einsum(
                "qgjk,kgd->qgjd",
                weights.astype(jnp.bfloat16),
                value_block,
                preferred_element_type=jnp.float32,
            )
            return (total_sum, mixed_out)

        is_live = (begin <= query_last) & (begin + block_len > prompt_first)
        return lax.cond(is_live, compute, lambda state_in: state_in, carry_state)

    pf_state = lax.fori_loop(0, piece_len // block_len, one_block, start_state)
    pf_attn = (
        (pf_state[1] / pf_state[0][..., None]).astype(jnp.bfloat16).reshape(pf_rows, q_heads * HEAD)
    )
    merged = tuple(
        (lax.dynamic_slice_in_dim(member, seq_index * dec_rows, dec_rows, 0) for member in combined)
    )
    own_rows = seq_index * dec_rows + jnp.arange(dec_rows, dtype=jnp.int32)
    own_query = lax.dynamic_slice_in_dim(dec_query, seq_index * dec_rows, dec_rows, 0).reshape(
        dec_rows, kv_heads, group_size, HEAD
    )
    near_ids = (own_rows // NEW)[:, None] * NEW + jnp.arange(NEW, dtype=jnp.int32)[None, :]
    near_keys = jnp.take(dec_key, near_ids, axis=0).reshape(dec_rows, NEW, kv_heads, HEAD)
    near_values = jnp.take(dec_value, near_ids, axis=0).reshape(dec_rows, NEW, kv_heads, HEAD)
    near_allowed = (jnp.arange(NEW, dtype=jnp.int32)[None, :] <= (own_rows % NEW)[:, None])[
        :, None, None, :
    ]
    near_scores = soft_cap(
        jnp.einsum("rgjd,rmgd->rgjm", own_query, near_keys, preferred_element_type=jnp.float32)
    )
    near_part = partial_softmax(near_scores, near_allowed, near_values, "rgjm,rmgd->rgjd")
    finished = combine(merged, near_part)
    dec_attn = (
        (finished[1] / finished[0][..., None])
        .astype(jnp.bfloat16)
        .reshape(dec_rows, q_heads * HEAD)
    )
    attn_rows = jnp.concatenate([pf_attn, dec_attn], axis=0)
    heads_all = lax.all_gather(attn_rows, "tp", axis=1, tiled=True)
    columns = heads_all
    projected = jnp.dot(
        columns,
        w_out,
        preferred_element_type=jnp.float32,
    )
    projected = projected.astype(jnp.bfloat16)
    return (projected[:pf_rows], projected[pf_rows:])


def solution(mesh):
    return jax.shard_map(
        shards,
        mesh=mesh,
        in_specs=(
            P("seq", None),
            P(),
            P(),
            P("seq", "tp"),
            P("seq", "tp"),
            P("seq", "tp"),
            P("seq", "tp"),
            P(),
            P(),
            P(),
            P(),
            P(None, "seq", "tp"),
            P(None, "seq", "tp"),
            P("seq", None, "tp"),
            P("seq", None, "tp"),
        ),
        out_specs=(P("seq", "tp"), P("seq", "tp")),
        check_vma=False,
    )
```

```python
import math

import jax
import jax.numpy as jnp
from jax import lax
from jax.sharding import PartitionSpec as P

HEAD = 128
SAMPLES = 16
NEW = 2


SOFTCAP = 50.0
QUERY_SCALE = 144.0 ** (-0.5)
NORM_EPSILON = 1e-06
ROPE_BASE = 10000.0


SEQ_AXES = ("sx", "sy", "sz")


def gather_seq(block):
    z_index = lax.axis_index("sz")
    other = lax.ppermute(block, "sz", perm=[(0, 1), (1, 0)])
    pair = jnp.where(z_index == 0, jnp.stack([block, other]), jnp.stack([other, block]))
    gathered = lax.all_gather(pair, ("sx", "sy"), axis=0)
    return gathered.reshape((-1,) + block.shape)


def rows_of(x, width):
    flat = x.reshape(-1).astype(jnp.bfloat16)
    tile = width * 16
    padded = -(-flat.shape[0] // tile) * tile
    return jnp.pad(flat, (0, padded - flat.shape[0])).reshape(-1, width)


def unrows(gathered, shape):
    count = gathered.shape[0]
    size = math.prod(shape)
    flat = gathered.reshape(count, -1)[:, :size].astype(jnp.float32)
    return jnp.sum(flat, axis=0).reshape(shape)


def rms_norm(inputs, norm_gain):
    values = inputs.astype(jnp.float32)
    mean_sq = jnp.mean(values * values, axis=-1, keepdims=True)
    return (values * lax.rsqrt(mean_sq + NORM_EPSILON) * norm_gain).astype(jnp.bfloat16)


def rotate(values, positions):
    half_size = values.shape[-1] // 2
    exponent = jnp.arange(half_size, dtype=jnp.float32) * (2.0 / values.shape[-1])
    frequency = ROPE_BASE ** (-exponent)
    angles = positions.astype(jnp.float32)[:, None] * frequency[None, :]
    cosine = jnp.cos(angles)[:, None, :]
    sine_part = jnp.sin(angles)[:, None, :]
    lower_half = values[..., :half_size]
    upper_half = values[..., half_size:]
    return jnp.concatenate(
        [
            lower_half * cosine - upper_half * sine_part,
            upper_half * cosine + lower_half * sine_part,
        ],
        axis=-1,
    )


def soft_cap(scores):
    return SOFTCAP * jnp.tanh(scores / SOFTCAP)


def prefill_positions(prefill_lengths, token_index):
    prompt_ends = jnp.cumsum(prefill_lengths)
    passed = token_index[:, None] >= prompt_ends[None, :]
    segment = jnp.sum(passed.astype(jnp.int32), axis=1)
    start_at = jnp.sum(jnp.where(passed, prefill_lengths[None, :], 0), axis=1)
    return (segment, token_index - start_at)


def lookup(table, indices):
    entries = jnp.arange(table.shape[0], dtype=jnp.int32)
    return jnp.sum(jnp.where(indices[:, None] == entries[None, :], table[None, :], 0), axis=1)


def combine(earlier, later):
    return (earlier[0] + later[0], earlier[1] + later[1])


def partial_softmax(scores, allowed, value_block, form):
    weights = jnp.where(allowed, jnp.exp(scores), 0.0)
    total_sum = jnp.sum(weights, axis=-1)
    mixed_out = jnp.einsum(
        form, weights.astype(jnp.bfloat16), value_block, preferred_element_type=jnp.float32
    )
    return (total_sum, mixed_out)


def shards(
    prefill_tokens,
    decode_tokens,
    norm_gain,
    w_query,
    w_key,
    w_value,
    w_output,
    prefill_lengths,
    context_lengths,
    tail_lengths,
    tail_slots,
    cache_keys,
    cache_values,
    tail_keys,
    tail_values,
):
    seq_count = lax.psum(1, SEQ_AXES)
    seq_index = lax.axis_index(SEQ_AXES)
    pf_rows = prefill_tokens.shape[0]
    dec_total = decode_tokens.shape[0]
    dec_rows = dec_total // seq_count
    q_heads = w_query.shape[1] // HEAD
    kv_heads = w_key.shape[1] // HEAD
    group_size = q_heads // kv_heads
    token_index = seq_index * pf_rows + jnp.arange(pf_rows, dtype=jnp.int32)
    query_seg, pf_positions = prefill_positions(prefill_lengths, token_index)
    row_ids = jnp.arange(dec_total, dtype=jnp.int32)
    sample_ids = row_ids // NEW
    dec_positions = (
        lookup(context_lengths, sample_ids // SAMPLES)
        + lookup(tail_lengths, sample_ids)
        + row_ids % NEW
    )
    positions = jnp.concatenate([pf_positions, dec_positions], axis=0)
    normed = rms_norm(jnp.concatenate([prefill_tokens, decode_tokens], axis=0), norm_gain)
    row_total = normed.shape[0]
    q_cols = w_query.shape[1]
    k_cols = w_key.shape[1]
    w_rows = w_query.shape[0]
    qkv_local = jnp.concatenate([w_query, w_key, w_value], axis=1)
    qkv_cols = qkv_local.shape[1]
    o_rows, o_cols = w_output.shape
    packed_w = jnp.concatenate([qkv_local, w_output.reshape(-1, qkv_cols)], axis=0)
    gathered_w = gather_seq(packed_w)
    w_qkv = gathered_w[:, :w_rows].reshape(seq_count * w_rows, qkv_cols)
    w_out = gathered_w[:, w_rows:].reshape(seq_count * o_rows, o_cols)
    qkv_all = jnp.dot(normed, w_qkv, preferred_element_type=jnp.float32)
    query_all = qkv_all[:, :q_cols]
    key_all = qkv_all[:, q_cols:q_cols + k_cols]
    value_all = qkv_all[:, q_cols + k_cols:]
    query_all = (
        rotate(query_all.reshape(row_total, q_heads, HEAD), positions) * QUERY_SCALE
    ).astype(jnp.bfloat16)
    key_all = (
        rotate(key_all.reshape(row_total, kv_heads, HEAD), positions)
        .astype(jnp.bfloat16)
        .reshape(row_total, -1)
    )
    value_all = value_all.astype(jnp.bfloat16)
    pf_query = query_all[:pf_rows].reshape(pf_rows, kv_heads, group_size, HEAD)
    pf_key = key_all[:pf_rows]
    pf_value = value_all[:pf_rows]
    dec_query = query_all[pf_rows:]
    dec_key = key_all[pf_rows:]
    dec_value = value_all[pf_rows:]
    prompt_count = cache_keys.shape[0]
    ctx_rows = cache_keys.shape[1]
    prompt_queries = dec_query.reshape(prompt_count, SAMPLES * NEW, kv_heads, group_size, HEAD)
    cache_k = cache_keys.reshape(prompt_count, ctx_rows, kv_heads, HEAD)
    cache_v = cache_values.reshape(prompt_count, ctx_rows, kv_heads, HEAD)
    cache_pos = seq_index * ctx_rows + jnp.arange(ctx_rows, dtype=jnp.int32)
    cache_allowed = (cache_pos[None, :] < context_lengths[:, None])[:, None, None, None, :]
    cache_scores = soft_cap(
        jnp.einsum("prgjd,pcgd->prgjc", prompt_queries, cache_k, preferred_element_type=jnp.float32)
    )
    prefix_part = partial_softmax(cache_scores, cache_allowed, cache_v, "prgjc,pcgd->prgjd")
    prefix_part = (
        prefix_part[0].reshape(dec_total, kv_heads, group_size),
        prefix_part[1].reshape(dec_total, kv_heads, group_size, HEAD),
    )
    slot_count = tail_keys.shape[0]
    tail_len = tail_keys.shape[1]
    sample_total = tail_slots.shape[0]
    local_slots = seq_index * slot_count + jnp.arange(slot_count, dtype=jnp.int32)
    owner = tail_slots[None, :] == local_slots[:, None]
    slot_queries = jnp.dot(
        owner.astype(jnp.bfloat16),
        dec_query.reshape(sample_total, NEW * q_heads * HEAD),
        preferred_element_type=jnp.float32,
    )
    slot_queries = slot_queries.astype(jnp.bfloat16).reshape(
        slot_count, NEW, kv_heads, group_size, HEAD
    )
    slot_lengths = jnp.sum(jnp.where(owner, tail_lengths[None, :], 0), axis=1)
    tail_allowed = (jnp.arange(tail_len, dtype=jnp.int32)[None, :] < slot_lengths[:, None])[
        :, None, None, None, :
    ]
    slot_keys = tail_keys.reshape(slot_count, tail_len, kv_heads, HEAD)
    slot_values = tail_values.reshape(slot_count, tail_len, kv_heads, HEAD)
    tail_scores = soft_cap(
        jnp.einsum("sngjd,stgd->sngjt", slot_queries, slot_keys, preferred_element_type=jnp.float32)
    )
    slot_part = partial_softmax(tail_scores, tail_allowed, slot_values, "sngjt,stgd->sngjd")
    owned_by = owner.T
    tail_sum = jnp.sum(jnp.where(owned_by[:, :, None, None, None], slot_part[0][None], 0.0), axis=1)
    tail_mix = jnp.sum(
        jnp.where(owned_by[:, :, None, None, None, None], slot_part[1][None], 0.0), axis=1
    )
    tail_part = (
        tail_sum.reshape(dec_total, kv_heads, group_size),
        tail_mix.reshape(dec_total, kv_heads, group_size, HEAD),
    )
    partials = combine(prefix_part, tail_part)
    kv_local = jnp.concatenate([pf_key, pf_value], axis=1)
    width = kv_local.shape[1]
    packed_kv = jnp.concatenate(
        [kv_local, rows_of(partials[1], width), rows_of(partials[0], width)], axis=0
    )
    gathered_kv = gather_seq(packed_kv)
    piece_len = pf_rows * seq_count
    key_piece = gathered_kv[:, :pf_rows, :k_cols].reshape(piece_len, k_cols)
    value_piece = gathered_kv[:, :pf_rows, k_cols:].reshape(piece_len, k_cols)
    mix_rows = rows_of(partials[1], width).shape[0]
    combined = (
        unrows(gathered_kv[:, pf_rows + mix_rows:], partials[0].shape),
        unrows(gathered_kv[:, pf_rows:pf_rows + mix_rows], partials[1].shape),
    )
    query_last = token_index[pf_rows - 1]
    prompt_first = token_index[0] - pf_positions[0]
    start_state = (
        jnp.zeros((pf_rows, kv_heads, group_size), jnp.float32),
        jnp.zeros((pf_rows, kv_heads, group_size, HEAD), jnp.float32),
    )
    block_len = math.gcd(512, piece_len)

    def one_block(block_step, carry_state):
        begin = block_step * block_len
        key_block = lax.dynamic_slice_in_dim(
            key_piece, block_step * block_len, block_len, 0
        ).reshape(block_len, kv_heads, HEAD)
        value_block = lax.dynamic_slice_in_dim(
            value_piece, block_step * block_len, block_len, 0
        ).reshape(block_len, kv_heads, HEAD)

        def compute(state_in):
            key_index = begin + jnp.arange(block_len, dtype=jnp.int32)
            key_seg, unused_pos = prefill_positions(prefill_lengths, key_index)
            allowed = (query_seg[:, None] == key_seg[None, :]) & (
                key_index[None, :] <= token_index[:, None]
            )
            scores = soft_cap(
                jnp.einsum(
                    "qgjd,kgd->qgjk", pf_query, key_block, preferred_element_type=jnp.float32
                )
            )
            weights = jnp.where(allowed[:, None, None, :], jnp.exp(scores), 0.0)
            total_sum = state_in[0] + jnp.sum(weights, axis=-1)
            mixed_out = state_in[1] + jnp.einsum(
                "qgjk,kgd->qgjd",
                weights.astype(jnp.bfloat16),
                value_block,
                preferred_element_type=jnp.float32,
            )
            return (total_sum, mixed_out)

        is_live = (begin <= query_last) & (begin + block_len > prompt_first)
        return lax.cond(is_live, compute, lambda state_in: state_in, carry_state)

    pf_state = lax.fori_loop(0, piece_len // block_len, one_block, start_state)
    pf_attn = (
        (pf_state[1] / pf_state[0][..., None]).astype(jnp.bfloat16).reshape(pf_rows, q_heads * HEAD)
    )
    merged = tuple(
        (lax.dynamic_slice_in_dim(member, seq_index * dec_rows, dec_rows, 0) for member in combined)
    )
    own_rows = seq_index * dec_rows + jnp.arange(dec_rows, dtype=jnp.int32)
    own_query = lax.dynamic_slice_in_dim(dec_query, seq_index * dec_rows, dec_rows, 0).reshape(
        dec_rows, kv_heads, group_size, HEAD
    )
    near_ids = (own_rows // NEW)[:, None] * NEW + jnp.arange(NEW, dtype=jnp.int32)[None, :]
    near_keys = jnp.take(dec_key, near_ids, axis=0).reshape(dec_rows, NEW, kv_heads, HEAD)
    near_values = jnp.take(dec_value, near_ids, axis=0).reshape(dec_rows, NEW, kv_heads, HEAD)
    near_allowed = (jnp.arange(NEW, dtype=jnp.int32)[None, :] <= (own_rows % NEW)[:, None])[
        :, None, None, :
    ]
    near_scores = soft_cap(
        jnp.einsum("rgjd,rmgd->rgjm", own_query, near_keys, preferred_element_type=jnp.float32)
    )
    near_part = partial_softmax(near_scores, near_allowed, near_values, "rgjm,rmgd->rgjd")
    finished = combine(merged, near_part)
    dec_attn = (
        (finished[1] / finished[0][..., None])
        .astype(jnp.bfloat16)
        .reshape(dec_rows, q_heads * HEAD)
    )
    attn_rows = jnp.concatenate([pf_attn, dec_attn], axis=0)
    heads_all = lax.all_gather(attn_rows, "tp", axis=1, tiled=True)
    columns = heads_all
    projected = jnp.dot(
        columns,
        w_out,
        preferred_element_type=jnp.float32,
    )
    projected = projected.astype(jnp.bfloat16)
    return (projected[:pf_rows], projected[pf_rows:])


def seq_split(mesh):
    column = mesh.devices[:, 0]
    try:
        xs = len({d.coords[0] for d in column})
        ys = len({d.coords[1] for d in column})
    except Exception:
        xs, ys = 4, 4
    return (xs, ys, column.shape[0] // (xs * ys))


def solution(mesh):
    split = seq_split(mesh)
    fine = jax.sharding.Mesh(
        mesh.devices.reshape(split + (mesh.devices.shape[1],)), SEQ_AXES + ("tp",)
    )
    seq = SEQ_AXES
    return jax.shard_map(
        shards,
        mesh=fine,
        in_specs=(
            P(seq, None),
            P(),
            P(),
            P(seq, "tp"),
            P(seq, "tp"),
            P(seq, "tp"),
            P(seq, "tp"),
            P(),
            P(),
            P(),
            P(),
            P(None, seq, "tp"),
            P(None, seq, "tp"),
            P(seq, None, "tp"),
            P(seq, None, "tp"),
        ),
        out_specs=(P(seq, "tp"), P(seq, "tp")),
        check_vma=False,
    )
```
